512 devices in a mesh: ctx: 16 (over y, x_hi, core), ch: 32 (over z, x_lo).
Axes of the slice: x: 4 (x_hi: 2, x_lo: 2; x = x_hi * 2 + x_lo), y: 4, z: 16, core: 2. Of those that a mesh axis runs over, the one named last changes fastest.
Arguments:
- query: bfloat16 [512, 16384], P('ch', 'ctx'), may hold values from -16 to 16
- key_branch: bfloat16 [512, 16384], P('ch', 'ctx'), may hold values from -6 to 6
- value_branch: bfloat16 [512, 16384], P('ch', 'ctx'), may hold values from -6 to 6
- residue: float32 [512, 16], P('ch'), may hold values from -1.5 to 1.5
- rate: float32 [512, 16], P('ch'), may hold values from 1.5258789e-05 to 0.03
- skip: float32 [512], P('ch'), may hold values from -4 to 4
- gain: float32 [512], P('ch'), may hold values from 0.1 to 1.9
Outputs:
- mixed_out: bfloat16 [512, 16384], P('ch', 'ctx')
The draws below stay inside these ranges and needn't reach their ends.
All inputs are finite; a program needn't handle non-finite values.
Results may differ from the reference program's by a relative error of at most 0.009.
Values may be sent and summed in bfloat16 or wider, within the bound.
No kernel may reach another device: no remote copies, remote signals or barrier semaphores. Data moves between devices by JAX's collectives and lax.ppermute only.
A program may use at most 64 MiB of HBM per device.

```python
import jax
import jax.numpy as jnp
from jax import lax

MODES = 16
CH = 512
SEQ = 16384


def draw_rate(key, part):
    picker = jax.random.uniform(jax.random.fold_in(key, 11), (CH, MODES))
    unit_draw = jax.random.uniform(jax.random.fold_in(key, 12), (CH, MODES))
    slow_share = 0.5
    slow_rate = jnp.exp(jnp.log(0.25 / SEQ) + unit_draw * jnp.log(8.0))
    fast_rate = jnp.exp(jnp.log(2.0 / SEQ) + unit_draw * (jnp.log(0.03) - jnp.log(2.0 / SEQ)))
    return jnp.where(picker < slow_share, slow_rate, fast_rate).astype(jnp.float32)


def draw_query(key, part):
    channel_pos = jnp.arange(CH, dtype=jnp.float32) / (CH - 1)
    base_vals = jax.random.truncated_normal(jax.random.fold_in(key, 22), -4.0, 4.0, (CH, SEQ))
    scales = 3.0 ** channel_pos
    return (base_vals * scales[:, None]).astype(jnp.bfloat16)


def block_levels(rng, dims, cuts, least, top_value):
    factor_of, own = 1.0, jax.random.fold_in(rng, 6)
    for dim, shards_of in cuts:
        steps = jnp.exp(jax.random.uniform(jax.random.fold_in(own, dim), (shards_of,), jnp.float32, least / len(cuts), top_value / len(cuts)))
        factor_of = factor_of * jnp.repeat(steps, dims[dim] // shards_of).reshape([-1 if axis == dim else 1 for axis in range(len(dims))])
    return factor_of


def scatter_about(rng, extent, width, bound, split=(), kind=jnp.bfloat16):
    values = width * jax.random.normal(rng, extent, jnp.float32)
    if split:
        values = values * block_levels(rng, extent, split, -0.22, 0.18)
    return jnp.clip(values, -bound, bound).astype(kind)


def setup_inputs(seed: int = 0) -> dict:
    seeds = jax.random.split(jax.random.key(seed), 8)
    query = draw_query(jax.random.fold_in(seeds[7], 71), 0)
    key_branch = scatter_about(seeds[1], (CH, SEQ), 1.0, 6.0, ((0, 32), (1, 16)))
    value_branch = scatter_about(seeds[2], (CH, SEQ), 1.0, 6.0, ((0, 32), (1, 16)))
    residue = scatter_about(seeds[3], (CH, MODES), MODES ** -0.5, 1.5, ((0, 32),), jnp.float32)
    rate = draw_rate(jax.random.fold_in(seeds[7], 71), 0)
    skip = scatter_about(seeds[5], (CH,), 1.0, 4.0, ((0, 32),), jnp.float32)
    gain = jnp.clip(1.0 + 0.18 * jax.random.normal(seeds[6], (CH,), jnp.float32), 0.1, 1.9)
    return {"query": query, "key_branch": key_branch, "value_branch": value_branch, "residue": residue, "rate": rate, "skip": skip, "gain": gain}


def modal_taps(lags, residue, rate):
    lag_float = jnp.maximum(lags, 0).astype(jnp.float32)
    scaled = jnp.sqrt(-jnp.expm1(-2.0 * rate)) * residue

    def add_mode(index, total):
        return total + scaled[:, index][:, None] * jnp.exp(-rate[:, index][:, None] * lag_float[None, :])
    start_total = jnp.zeros((residue.shape[0], lags.shape[0]), jnp.float32)
    total = lax.fori_loop(0, residue.shape[1], add_mode, start_total)
    return jnp.where((lags >= 0)[None, :], total, 0.0)

def reference(query, key_branch, value_branch, residue, rate, skip, gain):
    signal = (key_branch * value_branch).astype(jnp.bfloat16)
    lags = jnp.arange(SEQ, dtype=jnp.int32)
    taps = modal_taps(lags, residue, rate)
    signal_float = signal.astype(jnp.float32)
    spec_taps = jnp.fft.rfft(taps, n=2 * SEQ, axis=1)
    spec_signal = jnp.fft.rfft(signal_float, n=2 * SEQ, axis=1)
    conv = jnp.fft.irfft(spec_taps * spec_signal, n=2 * SEQ, axis=1)[:, :SEQ]
    mixed = query.astype(jnp.float32) * (conv + skip[:, None] * signal_float)
    mean_square = lax.optimization_barrier(jnp.mean(mixed * mixed, axis=0, keepdims=True))
    return (mixed / jnp.sqrt(mean_square + 1e-06) * gain[:, None]).astype(jnp.bfloat16)
```

```python
import jax
import jax.numpy as jnp
from jax import lax
from jax.sharding import PartitionSpec as P

HI = lax.Precision.HIGHEST
CHUNK = 128
CTX_MODE = "gather"
CH_MODE = "butterfly"


def shifted(block, axis, distance, cyclic=False):
    size = lax.axis_size(axis)
    if cyclic:
        route = [(i, (i + distance) % size) for i in range(size)]
    else:
        route = [(i, i + distance) for i in range(size) if i + distance < size]
    return lax.ppermute(block, axis, route)


def ctx_state(block_state, rate, block_len):
    count = lax.axis_size("ctx")
    position = lax.axis_index("ctx")
    if CTX_MODE == "gather":
        every = lax.all_gather(block_state, "ctx")
        earlier = jnp.arange(count)
        gap = jnp.maximum(position - 1 - earlier, 0).astype(jnp.float32)
        weight = jnp.exp(-rate[None] * block_len * gap[:, None, None])
        weight = jnp.where((earlier < position)[:, None, None], weight, 0.0)
        return jnp.sum(weight * every, axis=0)
    total = jnp.zeros_like(block_state)
    for distance in range(1, count):
        arrived = shifted(block_state, "ctx", distance)
        total = total + jnp.exp(-rate * (block_len * (distance - 1.0))) * arrived
    return total


def ch_sum(part):
    count = lax.axis_size("ch")
    if CH_MODE == "psum":
        return lax.psum(part, "ch")
    if CH_MODE == "butterfly":
        total = part
        step = 1
        while step < count:
            route = [(i, i ^ step) for i in range(count)]
            total = total + lax.ppermute(total, "ch", route)
            step *= 2
        return total
    total = part
    for distance in range(1, count):
        total = total + shifted(part, "ch", distance, cyclic=True)
    return total


def body(query, key_branch, value_branch, residue, rate, skip, gain):
    f32 = jnp.float32
    signal = (key_branch * value_branch).astype(jnp.bfloat16)
    sig = signal.astype(f32)
    rows, block_len = sig.shape
    chunk = min(CHUNK, block_len)
    chunks = block_len // chunk
    scaled = jnp.sqrt(-jnp.expm1(-2.0 * rate)) * residue
    lag = jnp.arange(chunk, dtype=f32)
    rate3 = rate[:, :, None]

    fall = scaled[:, :, None] * jnp.exp(-rate3 * lag)
    rise = jnp.exp(rate3 * lag)
    toeplitz = jnp.einsum("cmi,cmj->cij", fall, rise, precision=HI)
    toeplitz = jnp.where(lag[:, None] >= lag[None, :], toeplitz, 0.0)
    pieces = sig.reshape(rows, chunks, chunk)
    inner = jnp.einsum("ckj,cij->cki", pieces, toeplitz, precision=HI)

    tail = jnp.exp(-rate3 * (chunk - 1.0 - lag))
    ends = jnp.einsum("ckj,cmj->ckm", pieces, tail, precision=HI)
    later = jnp.arange(chunks + 1)[:, None]
    earlier = jnp.arange(chunks)[None, :]
    steps = jnp.maximum(later - 1 - earlier, 0).astype(f32)
    carry = jnp.exp(-rate[:, :, None, None] * (chunk * steps))
    carry = jnp.where(earlier < later, carry, 0.0)
    local = jnp.einsum("cmkq,cqm->ckm", carry, ends, precision=HI)
    block_state = local[:, chunks, :]

    before = ctx_state(block_state, rate, float(block_len))
    start = jnp.arange(chunks, dtype=f32)
    entering = jnp.exp(-rate[:, None, :] * (chunk * start)[None, :, None]) * before[:, None, :]
    entering = entering + local[:, :chunks, :]
    reach = scaled[:, :, None] * jnp.exp(-rate3 * (lag + 1.0))
    outer = jnp.einsum("ckm,cmi->cki", entering, reach, precision=HI)
    conv = (inner + outer).reshape(rows, block_len)

    mixed = query.astype(f32) * (conv + skip[:, None] * sig)
    channel_total = rows * lax.axis_size("ch")
    square_sum = ch_sum(jnp.sum(mixed * mixed, axis=0))
    mean_square = square_sum / channel_total
    return (mixed / jnp.sqrt(mean_square + 1e-06)[None, :] * gain[:, None]).astype(jnp.bfloat16)


def solution(mesh):
    placed = (
        P("ch", "ctx"),
        P("ch", "ctx"),
        P("ch", "ctx"),
        P("ch", None),
        P("ch", None),
        P("ch"),
        P("ch"),
    )
    return jax.shard_map(
        body, mesh=mesh, in_specs=placed, out_specs=P("ch", "ctx"), check_vma=False
    )
```

```python
import jax
import jax.numpy as jnp
from jax import lax
from jax.sharding import PartitionSpec as P

HI = lax.Precision.HIGHEST
CHUNK = 128
CTX_MODE = "a2a"
CH_MODE = "a2a"


def shifted(block, axis, distance, cyclic=False):
    size = lax.axis_size(axis)
    if cyclic:
        route = [(i, (i + distance) % size) for i in range(size)]
    else:
        route = [(i, i + distance) for i in range(size) if i + distance < size]
    return lax.ppermute(block, axis, route)


def everyone(block, axis):
    count = lax.axis_size(axis)
    copies = jnp.broadcast_to(block[None], (count,) + block.shape)
    return lax.all_to_all(copies, axis, 0, 0, tiled=True)


def ctx_state(block_state, rate, block_len):
    count = lax.axis_size("ctx")
    position = lax.axis_index("ctx")
    if CTX_MODE in ("gather", "a2a"):
        if CTX_MODE == "gather":
            every = lax.all_gather(block_state, "ctx")
        else:
            every = everyone(block_state, "ctx")
        earlier = jnp.arange(count)
        gap = jnp.maximum(position - 1 - earlier, 0).astype(jnp.float32)
        weight = jnp.exp(-rate[None] * block_len * gap[:, None, None])
        weight = jnp.where((earlier < position)[:, None, None], weight, 0.0)
        return jnp.sum(weight * every, axis=0)
    total = jnp.zeros_like(block_state)
    for distance in range(1, count):
        arrived = shifted(block_state, "ctx", distance)
        total = total + jnp.exp(-rate * (block_len * (distance - 1.0))) * arrived
    return total


def ch_sum(part):
    count = lax.axis_size("ch")
    if CH_MODE == "psum":
        return lax.psum(part, "ch")
    if CH_MODE == "a2a":
        return jnp.sum(everyone(part, "ch"), axis=0)
    if CH_MODE == "butterfly":
        total = part
        step = 1
        while step < count:
            route = [(i, i ^ step) for i in range(count)]
            total = total + lax.ppermute(total, "ch", route)
            step *= 2
        return total
    total = part
    for distance in range(1, count):
        total = total + shifted(part, "ch", distance, cyclic=True)
    return total


def body(query, key_branch, value_branch, residue, rate, skip, gain):
    f32 = jnp.float32
    signal = (key_branch * value_branch).astype(jnp.bfloat16)
    sig = signal.astype(f32)
    rows, block_len = sig.shape
    chunk = min(CHUNK, block_len)
    chunks = block_len // chunk
    scaled = jnp.sqrt(-jnp.expm1(-2.0 * rate)) * residue
    lag = jnp.arange(chunk, dtype=f32)
    rate3 = rate[:, :, None]

    fall = scaled[:, :, None] * jnp.exp(-rate3 * lag)
    rise = jnp.exp(rate3 * lag)
    toeplitz = jnp.einsum("cmi,cmj->cij", fall, rise, precision=HI)
    toeplitz = jnp.where(lag[:, None] >= lag[None, :], toeplitz, 0.0)
    pieces = sig.reshape(rows, chunks, chunk)
    inner = jnp.einsum("ckj,cij->cki", pieces, toeplitz, precision=HI)

    tail = jnp.exp(-rate3 * (chunk - 1.0 - lag))
    ends = jnp.einsum("ckj,cmj->ckm", pieces, tail, precision=HI)
    later = jnp.arange(chunks + 1)[:, None]
    earlier = jnp.arange(chunks)[None, :]
    steps = jnp.maximum(later - 1 - earlier, 0).astype(f32)
    carry = jnp.exp(-rate[:, :, None, None] * (chunk * steps))
    carry = jnp.where(earlier < later, carry, 0.0)
    local = jnp.einsum("cmkq,cqm->ckm", carry, ends, precision=HI)
    block_state = local[:, chunks, :]

    before = ctx_state(block_state, rate, float(block_len))
    start = jnp.arange(chunks, dtype=f32)
    entering = jnp.exp(-rate[:, None, :] * (chunk * start)[None, :, None]) * before[:, None, :]
    entering = entering + local[:, :chunks, :]
    reach = scaled[:, :, None] * jnp.exp(-rate3 * (lag + 1.0))
    outer = jnp.einsum("ckm,cmi->cki", entering, reach, precision=HI)
    conv = (inner + outer).reshape(rows, block_len)

    mixed = query.astype(f32) * (conv + skip[:, None] * sig)
    channel_total = rows * lax.axis_size("ch")
    square_sum = ch_sum(jnp.sum(mixed * mixed, axis=0))
    mean_square = square_sum / channel_total
    return (mixed / jnp.sqrt(mean_square + 1e-06)[None, :] * gain[:, None]).astype(jnp.bfloat16)


def solution(mesh):
    placed = (
        P("ch", "ctx"),
        P("ch", "ctx"),
        P("ch", "ctx"),
        P("ch", None),
        P("ch", None),
        P("ch"),
        P("ch"),
    )
    return jax.shard_map(
        body, mesh=mesh, in_specs=placed, out_specs=P("ch", "ctx"), check_vma=False
    )
```

```python
import jax
import jax.numpy as jnp
from jax import lax
from jax.sharding import PartitionSpec as P

HI = lax.Precision.HIGHEST
CHUNK = 128
CTX_MODE = "a2a"
CH_MODE = "a2a"
FLAT_STATE = True
CH_TYPE = jnp.bfloat16


def shifted(block, axis, distance, cyclic=False):
    size = lax.axis_size(axis)
    if cyclic:
        route = [(i, (i + distance) % size) for i in range(size)]
    else:
        route = [(i, i + distance) for i in range(size) if i + distance < size]
    return lax.ppermute(block, axis, route)


def everyone(block, axis):
    count = lax.axis_size(axis)
    copies = jnp.broadcast_to(block[None], (count,) + block.shape)
    return lax.all_to_all(copies, axis, 0, 0, tiled=True)


def ctx_state(block_state, rate, block_len):
    count = lax.axis_size("ctx")
    position = lax.axis_index("ctx")
    if CTX_MODE in ("gather", "a2a"):
        if CTX_MODE == "gather":
            every = lax.all_gather(block_state, "ctx")
        elif FLAT_STATE:
            rows, modes = block_state.shape
            every = everyone(block_state.reshape(rows * modes), "ctx")
            gap = jnp.maximum(position - 1 - jnp.arange(count), 0).astype(jnp.float32)
            weight = jnp.exp(-rate.reshape(1, rows * modes) * block_len * gap[:, None])
            weight = jnp.where((jnp.arange(count) < position)[:, None], weight, 0.0)
            return jnp.sum(weight * every, axis=0).reshape(rows, modes)
        else:
            every = everyone(block_state, "ctx")
        earlier = jnp.arange(count)
        gap = jnp.maximum(position - 1 - earlier, 0).astype(jnp.float32)
        weight = jnp.exp(-rate[None] * block_len * gap[:, None, None])
        weight = jnp.where((earlier < position)[:, None, None], weight, 0.0)
        return jnp.sum(weight * every, axis=0)
    total = jnp.zeros_like(block_state)
    for distance in range(1, count):
        arrived = shifted(block_state, "ctx", distance)
        total = total + jnp.exp(-rate * (block_len * (distance - 1.0))) * arrived
    return total


def ch_sum(part):
    count = lax.axis_size("ch")
    if CH_MODE == "psum":
        return lax.psum(part, "ch")
    if CH_MODE == "a2a":
        every = everyone(part.astype(CH_TYPE), "ch")
        return jnp.sum(every.astype(jnp.float32), axis=0)
    if CH_MODE == "butterfly":
        total = part
        step = 1
        while step < count:
            route = [(i, i ^ step) for i in range(count)]
            total = total + lax.ppermute(total, "ch", route)
            step *= 2
        return total
    total = part
    for distance in range(1, count):
        total = total + shifted(part, "ch", distance, cyclic=True)
    return total


def body(query, key_branch, value_branch, residue, rate, skip, gain):
    f32 = jnp.float32
    signal = (key_branch * value_branch).astype(jnp.bfloat16)
    sig = signal.astype(f32)
    rows, block_len = sig.shape
    chunk = min(CHUNK, block_len)
    chunks = block_len // chunk
    scaled = jnp.sqrt(-jnp.expm1(-2.0 * rate)) * residue
    lag = jnp.arange(chunk, dtype=f32)
    rate3 = rate[:, :, None]

    fall = scaled[:, :, None] * jnp.exp(-rate3 * lag)
    rise = jnp.exp(rate3 * lag)
    toeplitz = jnp.einsum("cmi,cmj->cij", fall, rise, precision=HI)
    toeplitz = jnp.where(lag[:, None] >= lag[None, :], toeplitz, 0.0)
    pieces = sig.reshape(rows, chunks, chunk)
    inner = jnp.einsum("ckj,cij->cki", pieces, toeplitz, precision=HI)

    tail = jnp.exp(-rate3 * (chunk - 1.0 - lag))
    ends = jnp.einsum("ckj,cmj->ckm", pieces, tail, precision=HI)
    later = jnp.arange(chunks + 1)[:, None]
    earlier = jnp.arange(chunks)[None, :]
    steps = jnp.maximum(later - 1 - earlier, 0).astype(f32)
    carry = jnp.exp(-rate[:, :, None, None] * (chunk * steps))
    carry = jnp.where(earlier < later, carry, 0.0)
    local = jnp.einsum("cmkq,cqm->ckm", carry, ends, precision=HI)
    block_state = local[:, chunks, :]

    before = ctx_state(block_state, rate, float(block_len))
    start = jnp.arange(chunks, dtype=f32)
    entering = jnp.exp(-rate[:, None, :] * (chunk * start)[None, :, None]) * before[:, None, :]
    entering = entering + local[:, :chunks, :]
    reach = scaled[:, :, None] * jnp.exp(-rate3 * (lag + 1.0))
    outer = jnp.einsum("ckm,cmi->cki", entering, reach, precision=HI)
    conv = (inner + outer).reshape(rows, block_len)

    mixed = query.astype(f32) * (conv + skip[:, None] * sig)
    channel_total = rows * lax.axis_size("ch")
    square_sum = ch_sum(jnp.sum(mixed * mixed, axis=0))
    mean_square = square_sum / channel_total
    return (mixed / jnp.sqrt(mean_square + 1e-06)[None, :] * gain[:, None]).astype(jnp.bfloat16)


def solution(mesh):
    placed = (
        P("ch", "ctx"),
        P("ch", "ctx"),
        P("ch", "ctx"),
        P("ch", None),
        P("ch", None),
        P("ch"),
        P("ch"),
    )
    return jax.shard_map(
        body, mesh=mesh, in_specs=placed, out_specs=P("ch", "ctx"), check_vma=False
    )
```

```python
import jax
import jax.numpy as jnp
from jax import lax
from jax.sharding import PartitionSpec as P

HI = lax.Precision.HIGHEST
CHUNK = 128
CTX_MODE = "a2a"
CH_MODE = "a2a"
FLAT_STATE = True
CH_TYPE = jnp.bfloat16


def shifted(block, axis, distance, cyclic=False):
    size = lax.axis_size(axis)
    if cyclic:
        route = [(i, (i + distance) % size) for i in range(size)]
    else:
        route = [(i, i + distance) for i in range(size) if i + distance < size]
    return lax.ppermute(block, axis, route)


def everyone(block, axis):
    count = lax.axis_size(axis)
    copies = jnp.broadcast_to(block[None], (count,) + block.shape)
    return lax.all_to_all(copies, axis, 0, 0, tiled=True)


def ctx_state(block_state, rate, block_len):
    count = lax.axis_size("ctx")
    position = lax.axis_index("ctx")
    if CTX_MODE in ("gather", "a2a"):
        if CTX_MODE == "gather":
            every = lax.all_gather(block_state, "ctx")
        elif FLAT_STATE:
            rows, modes = block_state.shape
            shape = (-1, 128) if (rows * modes) % 128 == 0 else (rows * modes,)
            every = everyone(block_state.reshape(shape), "ctx")
            every = every.reshape(count, rows * modes)
            gap = jnp.maximum(position - 1 - jnp.arange(count), 0).astype(jnp.float32)
            weight = jnp.exp(-rate.reshape(1, rows * modes) * block_len * gap[:, None])
            weight = jnp.where((jnp.arange(count) < position)[:, None], weight, 0.0)
            return jnp.sum(weight * every, axis=0).reshape(rows, modes)
        else:
            every = everyone(block_state, "ctx")
        earlier = jnp.arange(count)
        gap = jnp.maximum(position - 1 - earlier, 0).astype(jnp.float32)
        weight = jnp.exp(-rate[None] * block_len * gap[:, None, None])
        weight = jnp.where((earlier < position)[:, None, None], weight, 0.0)
        return jnp.sum(weight * every, axis=0)
    total = jnp.zeros_like(block_state)
    for distance in range(1, count):
        arrived = shifted(block_state, "ctx", distance)
        total = total + jnp.exp(-rate * (block_len * (distance - 1.0))) * arrived
    return total


def ch_sum(part):
    count = lax.axis_size("ch")
    if CH_MODE == "psum":
        return lax.psum(part, "ch")
    if CH_MODE == "a2a":
        if part.shape[0] % 128 == 0:
            every = everyone(part.astype(CH_TYPE).reshape(-1, 128), "ch")
            return jnp.sum(every.astype(jnp.float32), axis=0).reshape(part.shape)
        every = everyone(part.astype(CH_TYPE), "ch")
        return jnp.sum(every.astype(jnp.float32), axis=0)
    if CH_MODE == "butterfly":
        total = part
        step = 1
        while step < count:
            route = [(i, i ^ step) for i in range(count)]
            total = total + lax.ppermute(total, "ch", route)
            step *= 2
        return total
    total = part
    for distance in range(1, count):
        total = total + shifted(part, "ch", distance, cyclic=True)
    return total


def body(query, key_branch, value_branch, residue, rate, skip, gain):
    f32 = jnp.float32
    signal = (key_branch * value_branch).astype(jnp.bfloat16)
    sig = signal.astype(f32)
    rows, block_len = sig.shape
    chunk = min(CHUNK, block_len)
    chunks = block_len // chunk
    scaled = jnp.sqrt(-jnp.expm1(-2.0 * rate)) * residue
    lag = jnp.arange(chunk, dtype=f32)
    rate3 = rate[:, :, None]

    fall = scaled[:, :, None] * jnp.exp(-rate3 * lag)
    rise = jnp.exp(rate3 * lag)
    toeplitz = jnp.einsum("cmi,cmj->cij", fall, rise, precision=HI)
    toeplitz = jnp.where(lag[:, None] >= lag[None, :], toeplitz, 0.0)
    pieces = sig.reshape(rows, chunks, chunk)
    inner = jnp.einsum("ckj,cij->cki", pieces, toeplitz, precision=HI)

    tail = jnp.exp(-rate3 * (chunk - 1.0 - lag))
    ends = jnp.einsum("ckj,cmj->ckm", pieces, tail, precision=HI)
    later = jnp.arange(chunks + 1)[:, None]
    earlier = jnp.arange(chunks)[None, :]
    steps = jnp.maximum(later - 1 - earlier, 0).astype(f32)
    carry = jnp.exp(-rate[:, :, None, None] * (chunk * steps))
    carry = jnp.where(earlier < later, carry, 0.0)
    local = jnp.einsum("cmkq,cqm->ckm", carry, ends, precision=HI)
    block_state = local[:, chunks, :]

    before = ctx_state(block_state, rate, float(block_len))
    start = jnp.arange(chunks, dtype=f32)
    entering = jnp.exp(-rate[:, None, :] * (chunk * start)[None, :, None]) * before[:, None, :]
    entering = entering + local[:, :chunks, :]
    reach = scaled[:, :, None] * jnp.exp(-rate3 * (lag + 1.0))
    outer = jnp.einsum("ckm,cmi->cki", entering, reach, precision=HI)
    conv = (inner + outer).reshape(rows, block_len)

    mixed = query.astype(f32) * (conv + skip[:, None] * sig)
    channel_total = rows * lax.axis_size("ch")
    square_sum = ch_sum(jnp.sum(mixed * mixed, axis=0))
    mean_square = square_sum / channel_total
    return (mixed / jnp.sqrt(mean_square + 1e-06)[None, :] * gain[:, None]).astype(jnp.bfloat16)


def solution(mesh):
    placed = (
        P("ch", "ctx"),
        P("ch", "ctx"),
        P("ch", "ctx"),
        P("ch", None),
        P("ch", None),
        P("ch"),
        P("ch"),
    )
    return jax.shard_map(
        body, mesh=mesh, in_specs=placed, out_specs=P("ch", "ctx"), check_vma=False
    )
```

```python
import jax
import jax.numpy as jnp
from jax import lax
from jax.sharding import PartitionSpec as P

HI = lax.Precision.HIGHEST
CHUNK = 128
CTX_MODE = "a2a"
CH_MODE = "a2a"
FLAT_STATE = True
CH_TYPE = jnp.bfloat16
INNER_FIRST = False
GAIN_EARLY = True


def shifted(block, axis, distance, cyclic=False):
    size = lax.axis_size(axis)
    if cyclic:
        route = [(i, (i + distance) % size) for i in range(size)]
    else:
        route = [(i, i + distance) for i in range(size) if i + distance < size]
    return lax.ppermute(block, axis, route)


def everyone(block, axis):
    count = lax.axis_size(axis)
    copies = jnp.broadcast_to(block[None], (count,) + block.shape)
    return lax.all_to_all(copies, axis, 0, 0, tiled=True)


def ctx_state(block_state, rate, block_len):
    count = lax.axis_size("ctx")
    position = lax.axis_index("ctx")
    if CTX_MODE in ("gather", "a2a"):
        if CTX_MODE == "gather":
            every = lax.all_gather(block_state, "ctx")
        elif FLAT_STATE:
            rows, modes = block_state.shape
            shape = (-1, 128) if (rows * modes) % 128 == 0 else (rows * modes,)
            every = everyone(block_state.reshape(shape), "ctx")
            every = every.reshape(count, rows * modes)
            gap = jnp.maximum(position - 1 - jnp.arange(count), 0).astype(jnp.float32)
            weight = jnp.exp(-rate.reshape(1, rows * modes) * block_len * gap[:, None])
            weight = jnp.where((jnp.arange(count) < position)[:, None], weight, 0.0)
            return jnp.sum(weight * every, axis=0).reshape(rows, modes)
        else:
            every = everyone(block_state, "ctx")
        earlier = jnp.arange(count)
        gap = jnp.maximum(position - 1 - earlier, 0).astype(jnp.float32)
        weight = jnp.exp(-rate[None] * block_len * gap[:, None, None])
        weight = jnp.where((earlier < position)[:, None, None], weight, 0.0)
        return jnp.sum(weight * every, axis=0)
    total = jnp.zeros_like(block_state)
    for distance in range(1, count):
        arrived = shifted(block_state, "ctx", distance)
        total = total + jnp.exp(-rate * (block_len * (distance - 1.0))) * arrived
    return total


def ch_sum(part):
    count = lax.axis_size("ch")
    if CH_MODE == "psum":
        return lax.psum(part, "ch")
    if CH_MODE == "a2a":
        if part.shape[0] % 128 == 0:
            every = everyone(part.astype(CH_TYPE).reshape(-1, 128), "ch")
            return jnp.sum(every.astype(jnp.float32), axis=0).reshape(part.shape)
        every = everyone(part.astype(CH_TYPE), "ch")
        return jnp.sum(every.astype(jnp.float32), axis=0)
    if CH_MODE == "butterfly":
        total = part
        step = 1
        while step < count:
            route = [(i, i ^ step) for i in range(count)]
            total = total + lax.ppermute(total, "ch", route)
            step *= 2
        return total
    total = part
    for distance in range(1, count):
        total = total + shifted(part, "ch", distance, cyclic=True)
    return total


def body(query, key_branch, value_branch, residue, rate, skip, gain):
    f32 = jnp.float32
    signal = (key_branch * value_branch).astype(jnp.bfloat16)
    sig = signal.astype(f32)
    rows, block_len = sig.shape
    chunk = min(CHUNK, block_len)
    chunks = block_len // chunk
    scaled = jnp.sqrt(-jnp.expm1(-2.0 * rate)) * residue
    lag = jnp.arange(chunk, dtype=f32)
    rate3 = rate[:, :, None]

    fall = scaled[:, :, None] * jnp.exp(-rate3 * lag)
    rise = jnp.exp(rate3 * lag)
    toeplitz = jnp.einsum("cmi,cmj->cij", fall, rise, precision=HI)
    toeplitz = jnp.where(lag[:, None] >= lag[None, :], toeplitz, 0.0)
    pieces = sig.reshape(rows, chunks, chunk)
    inner = jnp.einsum("ckj,cij->cki", pieces, toeplitz, precision=HI)

    tail = jnp.exp(-rate3 * (chunk - 1.0 - lag))
    ends = jnp.einsum("ckj,cmj->ckm", pieces, tail, precision=HI)
    later = jnp.arange(chunks + 1)[:, None]
    earlier = jnp.arange(chunks)[None, :]
    steps = jnp.maximum(later - 1 - earlier, 0).astype(f32)
    carry = jnp.exp(-rate[:, :, None, None] * (chunk * steps))
    carry = jnp.where(earlier < later, carry, 0.0)
    local = jnp.einsum("cmkq,cqm->ckm", carry, ends, precision=HI)
    block_state = local[:, chunks, :]

    if INNER_FIRST:
        block_state, inner = lax.optimization_barrier((block_state, inner))
    before = ctx_state(block_state, rate, float(block_len))
    start = jnp.arange(chunks, dtype=f32)
    entering = jnp.exp(-rate[:, None, :] * (chunk * start)[None, :, None]) * before[:, None, :]
    entering = entering + local[:, :chunks, :]
    reach = scaled[:, :, None] * jnp.exp(-rate3 * (lag + 1.0))
    outer = jnp.einsum("ckm,cmi->cki", entering, reach, precision=HI)
    conv = (inner + outer).reshape(rows, block_len)

    mixed = query.astype(f32) * (conv + skip[:, None] * sig)
    channel_total = rows * lax.axis_size("ch")
    part = jnp.sum(mixed * mixed, axis=0)
    if GAIN_EARLY:
        weighted, part = lax.optimization_barrier((mixed * gain[:, None], part))
    square_sum = ch_sum(part)
    mean_square = square_sum / channel_total
    if GAIN_EARLY:
        return (weighted / jnp.sqrt(mean_square + 1e-06)[None, :]).astype(jnp.bfloat16)
    return (mixed / jnp.sqrt(mean_square + 1e-06)[None, :] * gain[:, None]).astype(jnp.bfloat16)


def solution(mesh):
    placed = (
        P("ch", "ctx"),
        P("ch", "ctx"),
        P("ch", "ctx"),
        P("ch", None),
        P("ch", None),
        P("ch"),
        P("ch"),
    )
    return jax.shard_map(
        body, mesh=mesh, in_specs=placed, out_specs=P("ch", "ctx"), check_vma=False
    )
```

```python
import jax
import jax.numpy as jnp
from jax import lax
from jax.sharding import PartitionSpec as P

HI = lax.Precision.HIGHEST
CHUNK = 128
CTX_MODE = "a2a"
CH_MODE = "a2a"
FLAT_STATE = True
CH_TYPE = jnp.bfloat16
INNER_FIRST = False
DIRECT_STATE = "sum"
GAIN_EARLY = True


def shifted(block, axis, distance, cyclic=False):
    size = lax.axis_size(axis)
    if cyclic:
        route = [(i, (i + distance) % size) for i in range(size)]
    else:
        route = [(i, i + distance) for i in range(size) if i + distance < size]
    return lax.ppermute(block, axis, route)


def everyone(block, axis):
    count = lax.axis_size(axis)
    copies = jnp.broadcast_to(block[None], (count,) + block.shape)
    return lax.all_to_all(copies, axis, 0, 0, tiled=True)


def ctx_state(block_state, rate, block_len):
    count = lax.axis_size("ctx")
    position = lax.axis_index("ctx")
    if CTX_MODE in ("gather", "a2a"):
        if CTX_MODE == "gather":
            every = lax.all_gather(block_state, "ctx")
        elif FLAT_STATE:
            rows, modes = block_state.shape
            shape = (-1, 128) if (rows * modes) % 128 == 0 else (rows * modes,)
            every = everyone(block_state.reshape(shape), "ctx")
            every = every.reshape(count, rows * modes)
            gap = jnp.maximum(position - 1 - jnp.arange(count), 0).astype(jnp.float32)
            weight = jnp.exp(-rate.reshape(1, rows * modes) * block_len * gap[:, None])
            weight = jnp.where((jnp.arange(count) < position)[:, None], weight, 0.0)
            return jnp.sum(weight * every, axis=0).reshape(rows, modes)
        else:
            every = everyone(block_state, "ctx")
        earlier = jnp.arange(count)
        gap = jnp.maximum(position - 1 - earlier, 0).astype(jnp.float32)
        weight = jnp.exp(-rate[None] * block_len * gap[:, None, None])
        weight = jnp.where((earlier < position)[:, None, None], weight, 0.0)
        return jnp.sum(weight * every, axis=0)
    total = jnp.zeros_like(block_state)
    for distance in range(1, count):
        arrived = shifted(block_state, "ctx", distance)
        total = total + jnp.exp(-rate * (block_len * (distance - 1.0))) * arrived
    return total


def ch_sum(part):
    count = lax.axis_size("ch")
    if CH_MODE == "psum":
        return lax.psum(part, "ch")
    if CH_MODE == "a2a":
        if part.shape[0] % 128 == 0:
            every = everyone(part.astype(CH_TYPE).reshape(-1, 128), "ch")
            return jnp.sum(every.astype(jnp.float32), axis=0).reshape(part.shape)
        every = everyone(part.astype(CH_TYPE), "ch")
        return jnp.sum(every.astype(jnp.float32), axis=0)
    if CH_MODE == "butterfly":
        total = part
        step = 1
        while step < count:
            route = [(i, i ^ step) for i in range(count)]
            total = total + lax.ppermute(total, "ch", route)
            step *= 2
        return total
    total = part
    for distance in range(1, count):
        total = total + shifted(part, "ch", distance, cyclic=True)
    return total


def body(query, key_branch, value_branch, residue, rate, skip, gain):
    f32 = jnp.float32
    signal = (key_branch * value_branch).astype(jnp.bfloat16)
    sig = signal.astype(f32)
    rows, block_len = sig.shape
    chunk = min(CHUNK, block_len)
    chunks = block_len // chunk
    scaled = jnp.sqrt(-jnp.expm1(-2.0 * rate)) * residue
    lag = jnp.arange(chunk, dtype=f32)
    rate3 = rate[:, :, None]

    fall = scaled[:, :, None] * jnp.exp(-rate3 * lag)
    rise = jnp.exp(rate3 * lag)
    toeplitz = jnp.einsum("cmi,cmj->cij", fall, rise, precision=HI)
    toeplitz = jnp.where(lag[:, None] >= lag[None, :], toeplitz, 0.0)
    pieces = sig.reshape(rows, chunks, chunk)
    inner = jnp.einsum("ckj,cij->cki", pieces, toeplitz, precision=HI)

    tail = jnp.exp(-rate3 * (chunk - 1.0 - lag))
    ends = jnp.einsum("ckj,cmj->ckm", pieces, tail, precision=HI)
    later = jnp.arange(chunks + 1)[:, None]
    earlier = jnp.arange(chunks)[None, :]
    steps = jnp.maximum(later - 1 - earlier, 0).astype(f32)
    carry = jnp.exp(-rate[:, :, None, None] * (chunk * steps))
    carry = jnp.where(earlier < later, carry, 0.0)
    local = jnp.einsum("cmkq,cqm->ckm", carry, ends, precision=HI)
    block_state = local[:, chunks, :]
    if DIRECT_STATE != "none":
        spot = jnp.arange(block_len, dtype=f32)
        decay = jnp.exp(-rate3 * (block_len - 1.0 - spot))
        if DIRECT_STATE == "sum":
            block_state = jnp.sum(sig[:, None, :] * decay, axis=2)
        else:
            block_state = jnp.einsum("cp,cmp->cm", sig, decay, precision=HI)

    if INNER_FIRST:
        block_state, inner = lax.optimization_barrier((block_state, inner))
    before = ctx_state(block_state, rate, float(block_len))
    start = jnp.arange(chunks, dtype=f32)
    entering = jnp.exp(-rate[:, None, :] * (chunk * start)[None, :, None]) * before[:, None, :]
    entering = entering + local[:, :chunks, :]
    reach = scaled[:, :, None] * jnp.exp(-rate3 * (lag + 1.0))
    outer = jnp.einsum("ckm,cmi->cki", entering, reach, precision=HI)
    conv = (inner + outer).reshape(rows, block_len)

    mixed = query.astype(f32) * (conv + skip[:, None] * sig)
    channel_total = rows * lax.axis_size("ch")
    part = jnp.sum(mixed * mixed, axis=0)
    if GAIN_EARLY:
        weighted, part = lax.optimization_barrier((mixed * gain[:, None], part))
    square_sum = ch_sum(part)
    mean_square = square_sum / channel_total
    if GAIN_EARLY:
        return (weighted / jnp.sqrt(mean_square + 1e-06)[None, :]).astype(jnp.bfloat16)
    return (mixed / jnp.sqrt(mean_square + 1e-06)[None, :] * gain[:, None]).astype(jnp.bfloat16)


def solution(mesh):
    placed = (
        P("ch", "ctx"),
        P("ch", "ctx"),
        P("ch", "ctx"),
        P("ch", None),
        P("ch", None),
        P("ch"),
        P("ch"),
    )
    return jax.shard_map(
        body, mesh=mesh, in_specs=placed, out_specs=P("ch", "ctx"), check_vma=False
    )
```
